128 devices in a mesh: sta: 64 (over x_hi, y, z, core), day: 2 (over x_lo).
Axes of the slice: x: 4 (x_hi: 2, x_lo: 2; x = x_hi * 2 + x_lo), y: 4, z: 4, core: 2. Of those that a mesh axis runs over, the one named last changes fastest.
Arguments:
- spectra: bfloat16 [2, 12, 2, 3072, 640], P('day', None, None, 'sta'), as said below
- window_valid: int32 [2, 12], replicated, may hold values 0 or 1
- owner_order: int32 [4], replicated, may hold values from 0 to 63
Outputs:
- correlations: bfloat16 [4, 48, 3072, 256], P(None, 'day', 'sta')
The draws below stay inside these ranges and needn't reach their ends.
Inputs may be any that keep to these rules, and one draw needn't show every extreme that they name: `spectra`: finite values.
All inputs are finite; a program needn't handle non-finite values.
Results may differ from the reference program's by a relative error of at most 0.0073.
Values may be sent and summed in bfloat16 or wider, within the bound.
No kernel may reach another device: no remote copies, remote signals or barrier semaphores. Data moves between devices by JAX's collectives and lax.ppermute only.
A program may use at most 192 MiB of HBM per device.

```python
import math
import jax
import jax.numpy as jnp
from jax import lax

WIN = 12
STEPS = 4
F = 640
LAGS = 256
NFFT = 2400
FIRST_BIN = 60
CH_DEV = 48
NCH = 3072
DAYS = 2
N_STA = 64


def draw_spectra(key, part):
    shape = (DAYS, WIN, 2, NCH, F)
    subkeys = jax.random.split(key, 3)
    values = jax.random.normal(subkeys[0], shape, jnp.float32)
    ceiling = math.log(10.0)
    row_scale = jnp.exp(jax.random.uniform(subkeys[1], (DAYS, WIN, 1, NCH, 1), jnp.float32, 0.0, ceiling))
    bin_scale = jnp.exp(jax.random.uniform(subkeys[2], (1, 1, 1, NCH, F), jnp.float32, 0.0, math.log(10.0)))
    return (values * row_scale * bin_scale).astype(jnp.bfloat16)


def place_ends(array, rng, least, high):
    place = [jax.random.randint(jax.random.fold_in(rng, axis), (), 0, length) for axis, length in enumerate(array.shape)]
    main_axis = array.shape.index(max(array.shape))
    next_to = place[:main_axis] + [(place[main_axis] + 1) % array.shape[main_axis]] + place[main_axis + 1:]
    return array.at[tuple(place)].set(least).at[tuple(next_to)].set(high)


def setup_inputs(seed: int = 0) -> dict:
    key_list = jax.random.split(jax.random.key(seed), 4)
    return {
        "spectra": draw_spectra(jax.random.fold_in(key_list[3], 71), 0),
        "window_valid": place_ends((jax.random.randint(key_list[1], (DAYS, WIN), 0, 4) < 3).astype(jnp.int32), jax.random.fold_in(key_list[1], 1), 0, 1),
        "owner_order": place_ends(jax.random.randint(key_list[2], (STEPS,), 0, N_STA), jax.random.fold_in(key_list[2], 1), 0, N_STA - 1).astype(jnp.int32),
    }


def whiten(spectra):
    values = spectra.astype(jnp.float32)
    energy = lax.optimization_barrier(jnp.mean(values * values, axis=(2, 4), keepdims=True))
    return (values / jnp.sqrt(energy + 1e-06)).astype(jnp.bfloat16)

def lag_table(bins, lag_count):
    freq_index = FIRST_BIN + lax.iota(jnp.int32, bins)
    lag_index = lax.iota(jnp.int32, lag_count) - lag_count // 2
    phase = freq_index[:, None] * lag_index[None, :] % NFFT
    angle = phase.astype(jnp.float32) * (2.0 * math.pi / NFFT)
    return jnp.stack([jnp.cos(angle), -jnp.sin(angle)]).astype(jnp.bfloat16)

def day_correlation(owner, local, day_valid, lag_grid, stack_scale):
    masked = owner * day_valid.astype(jnp.bfloat16)[:, None, None, None]
    turned = jnp.stack([local, jnp.concatenate([-local[:, 1:2], local[:, 0:1]], axis=1)], axis=2)
    cross = jnp.einsum('wcaf,wckbf->fakb', masked.astype(jnp.float32), turned.astype(jnp.float32))
    cross = (cross * stack_scale).astype(jnp.bfloat16)
    lag_sums = jnp.einsum('fakb,kft->abt', cross.astype(jnp.float32), lag_grid.astype(jnp.float32))
    return lag_sums * (1.0 / math.sqrt(cross.shape[0]))

def reference(spectra, window_valid, owner_order):
    white = whiten(spectra)
    lag_grid = lag_table(F, LAGS)
    stack_scale = 1.0 / math.sqrt(DAYS * WIN)

    def one_step(owner):
        owned = lax.dynamic_slice_in_dim(white, (owner * CH_DEV).astype(jnp.int32), CH_DEV, 3)

        def one_block(block):
            local = lax.dynamic_slice_in_dim(white, (block * CH_DEV).astype(jnp.int32), CH_DEV, 3)
            total = jnp.zeros((CH_DEV, CH_DEV, LAGS), jnp.float32)
            for day_index in range(DAYS):
                part = day_correlation(owned[day_index], local[day_index], window_valid[day_index], lag_grid, stack_scale)
                rounded = lax.optimization_barrier(part.astype(jnp.bfloat16))
                total = total + rounded.astype(jnp.float32)
            return total.astype(jnp.bfloat16)
        blocks = lax.map(one_block, lax.iota(jnp.int32, N_STA))
        return jnp.transpose(blocks, (1, 0, 2, 3)).reshape(CH_DEV, NCH, LAGS)
    return lax.map(one_step, owner_order)
```

```python
import math

import jax
import jax.numpy as jnp
from jax import lax
from jax.sharding import PartitionSpec as P

STEPS = 4
LAGS = 256
NFFT = 2400
FIRST_BIN = 60

PART_ORDERS = (
    ((0, 1, 3, 5, 2), 4),
    ((0, 3, 5, 1, 4), 2),
    ((0, 5, 1, 3, 2), 4),
)


def swap(value, bit, size):
    return lax.ppermute(value, "sta", [(i, i ^ (1 << bit)) for i in range(size)])


def halve(buf, order, me, size):
    for bit in order:
        v = (me >> bit) & 1
        keep = lax.dynamic_index_in_dim(buf, v, 0, keepdims=False)
        send = lax.dynamic_index_in_dim(buf, 1 - v, 0, keepdims=False)
        buf = keep + swap(send, bit, size)
    return buf


def double(piece, order, me, size):
    buf = piece
    for bit in reversed(order):
        v = (me >> bit) & 1
        other = swap(buf, bit, size)
        lo = jnp.where(v == 1, other, buf)
        hi = jnp.where(v == 1, buf, other)
        buf = jnp.stack([lo, hi], axis=0)
    return buf


def broadcast_blocks(whitened, owner_order):
    size = lax.axis_size("sta")
    me = lax.axis_index("sta")
    masked = jnp.stack(
        [jnp.where(me == owner_order[s], whitened, jnp.zeros_like(whitened)) for s in range(STEPS)]
    )
    shape = masked.shape
    planes = masked.reshape((-1,) + shape[-2:])
    parts = len(PART_ORDERS)
    per_part = planes.shape[0] // parts
    outs = []
    for p, (order, exch) in enumerate(PART_ORDERS):
        buf = planes[p * per_part:(p + 1) * per_part]
        buf = buf.reshape((2,) * len(order) + (-1,) + shape[-2:])
        piece = halve(buf, order, me, size)
        piece = piece + swap(piece, exch, size)
        full = double(piece, order, me, size)
        outs.append(full.reshape((per_part,) + shape[-2:]))
    return jnp.concatenate(outs, axis=0).reshape(shape)


def whiten(spectra):
    values = spectra.astype(jnp.float32)
    energy = jnp.mean(values * values, axis=(2, 4), keepdims=True)
    return (values / jnp.sqrt(energy + 1e-06)).astype(jnp.bfloat16)


def lag_table(bins, lag_count):
    freq_index = FIRST_BIN + lax.iota(jnp.int32, bins)
    lag_index = lax.iota(jnp.int32, lag_count) - lag_count // 2
    phase = freq_index[:, None] * lag_index[None, :] % NFFT
    angle = phase.astype(jnp.float32) * (2.0 * math.pi / NFFT)
    return jnp.stack([jnp.cos(angle), -jnp.sin(angle)]).astype(jnp.bfloat16)


def day_correlation(owner, local, day_valid, lag_grid, stack_scale):
    masked = owner * day_valid.astype(jnp.bfloat16)[:, None, None, None]
    turned = jnp.stack([local, jnp.concatenate([-local[:, 1:2], local[:, 0:1]], axis=1)], axis=2)
    cross = jnp.einsum("wcaf,wckbf->fakb", masked, turned, preferred_element_type=jnp.float32)
    cross = (cross * stack_scale).astype(jnp.bfloat16)
    lag_sums = jnp.einsum("fakb,kft->abt", cross, lag_grid, preferred_element_type=jnp.float32)
    return lag_sums * (1.0 / math.sqrt(cross.shape[0]))


def body(spectra, window_valid, owner_order):
    day_index = lax.axis_index("day")
    whitened = whiten(spectra)[0]
    lag_grid = lag_table(whitened.shape[3], LAGS)
    stack_scale = 1.0 / math.sqrt(lax.axis_size("day") * whitened.shape[0])
    own_valid = lax.dynamic_index_in_dim(window_valid, day_index, 0, keepdims=False)
    owners = broadcast_blocks(whitened, owner_order)
    results = []
    for step_index in range(STEPS):
        lag_sums = day_correlation(owners[step_index], whitened, own_valid, lag_grid, stack_scale)
        share = lax.psum_scatter(
            lag_sums.astype(jnp.bfloat16), "day", scatter_dimension=0, tiled=True
        )
        results.append(share)
    return jnp.stack(results)


def solution(mesh):
    return jax.shard_map(
        body,
        mesh=mesh,
        in_specs=(P("day", None, None, "sta", None), P(), P()),
        out_specs=P(None, "day", "sta", None),
        check_vma=False,
    )
```

```python
import math

import jax
import jax.numpy as jnp
from jax import lax
from jax.sharding import PartitionSpec as P

STEPS = 4
LAGS = 256
NFFT = 2400
FIRST_BIN = 60

PART_ORDERS = (
    ((0, 1, 3, 5, 2), 4),
    ((0, 3, 5, 1, 4), 2),
    ((0, 5, 1, 3, 2), 4),
)


def swap(value, bit, size):
    return lax.ppermute(value, "sta", [(i, i ^ (1 << bit)) for i in range(size)])


def halve(buf, order, me, size):
    for bit in order:
        v = (me >> bit) & 1
        keep = lax.dynamic_index_in_dim(buf, v, 0, keepdims=False)
        send = lax.dynamic_index_in_dim(buf, 1 - v, 0, keepdims=False)
        buf = keep + swap(send, bit, size)
    return buf


def double(piece, order, me, size):
    buf = piece
    for bit in reversed(order):
        v = (me >> bit) & 1
        other = swap(buf, bit, size)
        lo = jnp.where(v == 1, other, buf)
        hi = jnp.where(v == 1, buf, other)
        buf = jnp.stack([lo, hi], axis=0)
    return buf


def broadcast_blocks(whitened, owner_order):
    size = lax.axis_size("sta")
    me = lax.axis_index("sta")
    masked = jnp.stack(
        [jnp.where(me == owner_order[s], whitened, jnp.zeros_like(whitened)) for s in range(STEPS)]
    )
    shape = masked.shape
    planes = masked.reshape((-1,) + shape[-2:])
    parts = len(PART_ORDERS)
    per_part = planes.shape[0] // parts
    outs = []
    for p, (order, exch) in enumerate(PART_ORDERS):
        buf = planes[p * per_part:(p + 1) * per_part]
        buf = buf.reshape((2,) * len(order) + (-1,) + shape[-2:])
        piece = halve(buf, order, me, size)
        piece = piece + swap(piece, exch, size)
        full = double(piece, order, me, size)
        outs.append(full.reshape((per_part,) + shape[-2:]))
    return jnp.concatenate(outs, axis=0).reshape(shape)


def whiten(spectra):
    values = spectra.astype(jnp.float32)
    energy = jnp.mean(values * values, axis=(2, 4), keepdims=True)
    return (values / jnp.sqrt(energy + 1e-06)).astype(jnp.bfloat16)


def lag_table(bins, lag_count):
    freq_index = FIRST_BIN + lax.iota(jnp.int32, bins)
    lag_index = lax.iota(jnp.int32, lag_count) - lag_count // 2
    phase = freq_index[:, None] * lag_index[None, :] % NFFT
    angle = phase.astype(jnp.float32) * (2.0 * math.pi / NFFT)
    return jnp.stack([jnp.cos(angle), -jnp.sin(angle)]).astype(jnp.bfloat16)


def day_correlation(owner, local, day_valid, lag_grid, stack_scale):
    masked = owner * day_valid.astype(jnp.bfloat16)[:, None, None, None]
    turned = jnp.concatenate([masked[:, 1:2], -masked[:, 0:1]], axis=1)
    wide = local.astype(jnp.float32)[:, :, None, :, :]
    real = jnp.sum(masked.astype(jnp.float32)[:, :, :, None, :] * wide, axis=(0, 1))
    imag = jnp.sum(turned.astype(jnp.float32)[:, :, :, None, :] * wide, axis=(0, 1))
    cross = jnp.concatenate([real, imag], axis=-1)
    cross = (cross * stack_scale).astype(jnp.bfloat16)
    a, b, kf = cross.shape
    lag_sums = jnp.dot(
        cross.reshape(a * b, kf), lag_grid.reshape(kf, -1), preferred_element_type=jnp.float32
    ).reshape(a, b, -1)
    return lag_sums * (1.0 / math.sqrt(kf // 2))


def body(spectra, window_valid, owner_order):
    day_index = lax.axis_index("day")
    whitened = whiten(spectra)[0]
    lag_grid = lag_table(whitened.shape[3], LAGS)
    stack_scale = 1.0 / math.sqrt(lax.axis_size("day") * whitened.shape[0])
    own_valid = lax.dynamic_index_in_dim(window_valid, day_index, 0, keepdims=False)
    owners = broadcast_blocks(whitened, owner_order)
    results = []
    for step_index in range(STEPS):
        lag_sums = day_correlation(owners[step_index], whitened, own_valid, lag_grid, stack_scale)
        share = lax.psum_scatter(
            lag_sums.astype(jnp.bfloat16), "day", scatter_dimension=0, tiled=True
        )
        results.append(share)
    return jnp.stack(results)


def solution(mesh):
    return jax.shard_map(
        body,
        mesh=mesh,
        in_specs=(P("day", None, None, "sta", None), P(), P()),
        out_specs=P(None, "day", "sta", None),
        check_vma=False,
    )
```

```python
import math

import jax
import jax.numpy as jnp
from jax import lax
from jax.sharding import PartitionSpec as P

STEPS = 4
LAGS = 256
NFFT = 2400
FIRST_BIN = 60

PART_ORDERS = (
    ((0, 1, 3, 5, 2), 4),
    ((0, 3, 5, 1, 4), 2),
    ((0, 5, 1, 3, 2), 4),
)


def swap(value, bit, size):
    return lax.ppermute(value, "sta", [(i, i ^ (1 << bit)) for i in range(size)])


def halve(buf, order, me, size):
    for bit in order:
        v = (me >> bit) & 1
        keep = lax.dynamic_index_in_dim(buf, v, 0, keepdims=False)
        send = lax.dynamic_index_in_dim(buf, 1 - v, 0, keepdims=False)
        buf = keep + swap(send, bit, size)
    return buf


def double(piece, order, me, size):
    buf = piece
    for bit in reversed(order):
        v = (me >> bit) & 1
        other = swap(buf, bit, size)
        lo = jnp.where(v == 1, other, buf)
        hi = jnp.where(v == 1, buf, other)
        buf = jnp.stack([lo, hi], axis=0)
    return buf


def broadcast_blocks(whitened, owner_order):
    size = lax.axis_size("sta")
    me = lax.axis_index("sta")
    masked = jnp.stack(
        [jnp.where(me == owner_order[s], whitened, jnp.zeros_like(whitened)) for s in range(STEPS)]
    )
    shape = masked.shape
    planes = masked.reshape((-1,) + shape[-2:])
    parts = len(PART_ORDERS)
    per_part = planes.shape[0] // parts
    outs = []
    for p, (order, exch) in enumerate(PART_ORDERS):
        buf = planes[p * per_part:(p + 1) * per_part]
        buf = buf.reshape((2,) * len(order) + (-1,) + shape[-2:])
        piece = halve(buf, order, me, size)
        piece = piece + swap(piece, exch, size)
        full = double(piece, order, me, size)
        outs.append(full.reshape((per_part,) + shape[-2:]))
    return jnp.concatenate(outs, axis=0).reshape(shape)


def whiten(spectra):
    values = spectra.astype(jnp.float32)
    energy = jnp.mean(values * values, axis=(2, 4), keepdims=True)
    return (values / jnp.sqrt(energy + 1e-06)).astype(jnp.bfloat16)


def lag_table(bins, lag_count):
    freq_index = FIRST_BIN + lax.iota(jnp.int32, bins)
    lag_index = lax.iota(jnp.int32, lag_count) - lag_count // 2
    phase = freq_index[:, None] * lag_index[None, :] % NFFT
    angle = phase.astype(jnp.float32) * (2.0 * math.pi / NFFT)
    return jnp.stack([jnp.cos(angle), -jnp.sin(angle)]).astype(jnp.bfloat16)


def day_correlation(owner, local, day_valid, lag_grid, stack_scale):
    masked = owner * day_valid.astype(jnp.bfloat16)[:, None, None, None]
    turned = jnp.concatenate([masked[:, 1:2], -masked[:, 0:1]], axis=1)
    wide = local.astype(jnp.float32)[:, :, None, :, :]
    real = jnp.sum(masked.astype(jnp.float32)[:, :, :, None, :] * wide, axis=(0, 1))
    imag = jnp.sum(turned.astype(jnp.float32)[:, :, :, None, :] * wide, axis=(0, 1))
    cross = jnp.concatenate([real, imag], axis=-1)
    cross = (cross * stack_scale).astype(jnp.bfloat16)
    a, b, kf = cross.shape
    lag_sums = jnp.dot(
        cross.reshape(a * b, kf), lag_grid.reshape(kf, -1), preferred_element_type=jnp.float32
    ).reshape(a, b, -1)
    return lag_sums * (1.0 / math.sqrt(kf // 2))


def body(spectra, window_valid, owner_order):
    day_index = lax.axis_index("day")
    whitened = whiten(spectra)[0]
    lag_grid = lag_table(whitened.shape[3], LAGS)
    stack_scale = 1.0 / math.sqrt(lax.axis_size("day") * whitened.shape[0])
    own_valid = lax.dynamic_index_in_dim(window_valid, day_index, 0, keepdims=False)
    owners = broadcast_blocks(whitened, owner_order)
    results = []
    local = whitened
    for step_index in range(STEPS):
        if step_index >= 2:
            local, results[step_index - 2] = lax.optimization_barrier((local, results[step_index - 2]))
        lag_sums = day_correlation(owners[step_index], local, own_valid, lag_grid, stack_scale)
        lag_sums, local = lax.optimization_barrier((lag_sums, local))
        share = lax.psum_scatter(
            lag_sums.astype(jnp.bfloat16), "day", scatter_dimension=0, tiled=True
        )
        results.append(share)
    return jnp.stack(results)


def solution(mesh):
    return jax.shard_map(
        body,
        mesh=mesh,
        in_specs=(P("day", None, None, "sta", None), P(), P()),
        out_specs=P(None, "day", "sta", None),
        check_vma=False,
    )
```

```python
import math

import jax
import jax.numpy as jnp
from jax import lax
from jax.sharding import PartitionSpec as P

STEPS = 4
LAGS = 256
NFFT = 2400
FIRST_BIN = 60

PART_ORDERS = (
    ((0, 1, 3, 5, 2), 4),
    ((0, 3, 5, 1, 4), 2),
    ((0, 5, 1, 3, 2), 4),
)


def swap(value, bit, size):
    return lax.ppermute(value, "sta", [(i, i ^ (1 << bit)) for i in range(size)])


def halve(buf, order, me, size):
    for bit in order:
        v = (me >> bit) & 1
        keep = lax.dynamic_index_in_dim(buf, v, 0, keepdims=False)
        send = lax.dynamic_index_in_dim(buf, 1 - v, 0, keepdims=False)
        buf = keep + swap(send, bit, size)
    return buf


def double(piece, order, me, size):
    buf = piece
    for bit in reversed(order):
        v = (me >> bit) & 1
        other = swap(buf, bit, size)
        lo = jnp.where(v == 1, other, buf)
        hi = jnp.where(v == 1, buf, other)
        buf = jnp.stack([lo, hi], axis=0)
    return buf


def broadcast_blocks(whitened, owner_order):
    size = lax.axis_size("sta")
    me = lax.axis_index("sta")
    masked = jnp.stack(
        [jnp.where(me == owner_order[s], whitened, jnp.zeros_like(whitened)) for s in range(STEPS)]
    )
    shape = masked.shape
    planes = masked.reshape((-1,) + shape[-2:])
    parts = len(PART_ORDERS)
    per_part = planes.shape[0] // parts
    outs = []
    for p, (order, exch) in enumerate(PART_ORDERS):
        buf = planes[p * per_part:(p + 1) * per_part]
        buf = buf.reshape((2,) * len(order) + (-1,) + shape[-2:])
        piece = halve(buf, order, me, size)
        piece = piece + swap(piece, exch, size)
        full = double(piece, order, me, size)
        outs.append(full.reshape((per_part,) + shape[-2:]))
    return jnp.concatenate(outs, axis=0).reshape(shape)


def whiten(spectra):
    values = spectra.astype(jnp.float32)
    energy = jnp.mean(values * values, axis=(2, 4), keepdims=True)
    return (values / jnp.sqrt(energy + 1e-06)).astype(jnp.bfloat16)


def lag_table(bins, lag_count):
    freq_index = FIRST_BIN + lax.iota(jnp.int32, bins)
    lag_index = lax.iota(jnp.int32, lag_count) - lag_count // 2
    phase = freq_index[:, None] * lag_index[None, :] % NFFT
    angle = phase.astype(jnp.float32) * (2.0 * math.pi / NFFT)
    return jnp.stack([jnp.cos(angle), -jnp.sin(angle)]).astype(jnp.bfloat16)


def day_correlation(owner, local, day_valid, lag_grid, stack_scale):
    masked = owner * day_valid.astype(jnp.bfloat16)[:, None, None, None]
    turned = jnp.concatenate([masked[:, 1:2], -masked[:, 0:1]], axis=1)
    wide = local.astype(jnp.float32)[:, :, None, :, :]
    real = jnp.sum(masked.astype(jnp.float32)[:, :, :, None, :] * wide, axis=(0, 1))
    imag = jnp.sum(turned.astype(jnp.float32)[:, :, :, None, :] * wide, axis=(0, 1))
    cross = jnp.concatenate([real, imag], axis=-1)
    cross = (cross * stack_scale).astype(jnp.bfloat16)
    a, b, kf = cross.shape
    lag_sums = jnp.dot(
        cross.reshape(a * b, kf), lag_grid.reshape(kf, -1), preferred_element_type=jnp.float32
    ).reshape(a, b, -1)
    return lag_sums * (1.0 / math.sqrt(kf // 2))


def body(spectra, window_valid, owner_order):
    day_index = lax.axis_index("day")
    whitened = whiten(spectra)[0]
    lag_grid = lag_table(whitened.shape[3], LAGS)
    stack_scale = 1.0 / math.sqrt(lax.axis_size("day") * whitened.shape[0])
    own_valid = lax.dynamic_index_in_dim(window_valid, day_index, 0, keepdims=False)
    owners = broadcast_blocks(whitened, owner_order)
    half = whitened.shape[2] // lax.axis_size("day")
    partner = [(0, 1), (1, 0)]
    results = []
    local = whitened
    for step_index in range(STEPS):
        if results:
            local, results[-1] = lax.optimization_barrier((local, results[-1]))
        owner = owners[step_index]
        theirs = lax.dynamic_slice_in_dim(owner, (1 - day_index) * half, half, 2)
        sent = day_correlation(theirs, local, own_valid, lag_grid, stack_scale).astype(jnp.bfloat16)
        sent, local = lax.optimization_barrier((sent, local))
        received = lax.ppermute(sent, "day", partner)
        mine = lax.dynamic_slice_in_dim(owner, day_index * half, half, 2)
        kept = day_correlation(mine, local, own_valid, lag_grid, stack_scale).astype(jnp.bfloat16)
        kept, local = lax.optimization_barrier((kept, local))
        share = (kept.astype(jnp.float32) + received.astype(jnp.float32)).astype(jnp.bfloat16)
        results.append(share)
    return jnp.stack(results)


def solution(mesh):
    return jax.shard_map(
        body,
        mesh=mesh,
        in_specs=(P("day", None, None, "sta", None), P(), P()),
        out_specs=P(None, "day", "sta", None),
        check_vma=False,
    )
```

```python
import math

import jax
import jax.numpy as jnp
from jax import lax
from jax.sharding import PartitionSpec as P

STEPS = 4
LAGS = 256
NFFT = 2400
FIRST_BIN = 60

PART_ORDERS = (
    ((0, 1, 3, 5, 2), 4),
    ((0, 3, 5, 1, 4), 2),
    ((0, 5, 1, 3, 2), 4),
)


def swap(value, bit, size):
    return lax.ppermute(value, "sta", [(i, i ^ (1 << bit)) for i in range(size)])


def halve(buf, order, me, size):
    for bit in order:
        v = (me >> bit) & 1
        keep = lax.dynamic_index_in_dim(buf, v, 0, keepdims=False)
        send = lax.dynamic_index_in_dim(buf, 1 - v, 0, keepdims=False)
        buf = keep + swap(send, bit, size)
    return buf


def double(piece, order, me, size):
    buf = piece
    for bit in reversed(order):
        v = (me >> bit) & 1
        other = swap(buf, bit, size)
        lo = jnp.where(v == 1, other, buf)
        hi = jnp.where(v == 1, buf, other)
        buf = jnp.stack([lo, hi], axis=0)
    return buf


def broadcast_blocks(whitened, owner_order):
    size = lax.axis_size("sta")
    me = lax.axis_index("sta")
    masked = jnp.stack(
        [jnp.where(me == owner_order[s], whitened, jnp.zeros_like(whitened)) for s in range(STEPS)]
    )
    shape = masked.shape
    planes = masked.reshape((-1,) + shape[-2:])
    parts = len(PART_ORDERS)
    per_part = planes.shape[0] // parts
    outs = []
    for p, (order, exch) in enumerate(PART_ORDERS):
        buf = planes[p * per_part:(p + 1) * per_part]
        buf = buf.reshape((2,) * len(order) + (-1,) + shape[-2:])
        piece = halve(buf, order, me, size)
        piece = piece + swap(piece, exch, size)
        full = double(piece, order, me, size)
        outs.append(full.reshape((per_part,) + shape[-2:]))
    return jnp.concatenate(outs, axis=0).reshape(shape)


def whiten(spectra):
    values = spectra.astype(jnp.float32)
    energy = jnp.mean(values * values, axis=(2, 4), keepdims=True)
    return (values / jnp.sqrt(energy + 1e-06)).astype(jnp.bfloat16)


def lag_table(bins, lag_count):
    freq_index = FIRST_BIN + lax.iota(jnp.int32, bins)
    lag_index = lax.iota(jnp.int32, lag_count) - lag_count // 2
    phase = freq_index[:, None] * lag_index[None, :] % NFFT
    angle = phase.astype(jnp.float32) * (2.0 * math.pi / NFFT)
    return jnp.stack([jnp.cos(angle), -jnp.sin(angle)]).astype(jnp.bfloat16)


def split_local(local):
    wide = local.astype(jnp.float32)
    return wide[:, 0], wide[:, 1], wide[:, 0] - wide[:, 1]


def day_correlation(owner, local_parts, day_valid, lag_grid, stack_scale):
    real_l, imag_l, diff_l = local_parts
    masked = (owner * day_valid.astype(jnp.bfloat16)[:, None, None, None]).astype(jnp.float32)
    real_o, imag_o = masked[:, 0], masked[:, 1]
    sum_o = real_o + imag_o
    p = jnp.sum(real_o[:, :, None, :] * real_l[:, None, :, :], axis=0)
    q = jnp.sum(imag_o[:, :, None, :] * imag_l[:, None, :, :], axis=0)
    r = jnp.sum(sum_o[:, :, None, :] * diff_l[:, None, :, :], axis=0)
    cross = jnp.concatenate([p + q, (r - p) + q], axis=-1)
    cross = (cross * stack_scale).astype(jnp.bfloat16)
    a, b, kf = cross.shape
    lag_sums = jnp.dot(
        cross.reshape(a * b, kf), lag_grid.reshape(kf, -1), preferred_element_type=jnp.float32
    ).reshape(a, b, -1)
    return lag_sums * (1.0 / math.sqrt(kf // 2))


def body(spectra, window_valid, owner_order):
    day_index = lax.axis_index("day")
    whitened = whiten(spectra)[0]
    lag_grid = lag_table(whitened.shape[3], LAGS)
    stack_scale = 1.0 / math.sqrt(lax.axis_size("day") * whitened.shape[0])
    own_valid = lax.dynamic_index_in_dim(window_valid, day_index, 0, keepdims=False)
    owners = broadcast_blocks(whitened, owner_order)
    half = whitened.shape[2] // lax.axis_size("day")
    partner = [(0, 1), (1, 0)]
    results = []
    local = split_local(whitened)
    for step_index in range(STEPS):
        if results:
            local, results[-1] = lax.optimization_barrier((local, results[-1]))
        owner = owners[step_index]
        theirs = lax.dynamic_slice_in_dim(owner, (1 - day_index) * half, half, 2)
        sent = day_correlation(theirs, local, own_valid, lag_grid, stack_scale).astype(jnp.bfloat16)
        sent, local = lax.optimization_barrier((sent, local))
        received = lax.ppermute(sent, "day", partner)
        mine = lax.dynamic_slice_in_dim(owner, day_index * half, half, 2)
        kept = day_correlation(mine, local, own_valid, lag_grid, stack_scale).astype(jnp.bfloat16)
        kept, local = lax.optimization_barrier((kept, local))
        share = (kept.astype(jnp.float32) + received.astype(jnp.float32)).astype(jnp.bfloat16)
        results.append(share)
    return jnp.stack(results)


def solution(mesh):
    return jax.shard_map(
        body,
        mesh=mesh,
        in_specs=(P("day", None, None, "sta", None), P(), P()),
        out_specs=P(None, "day", "sta", None),
        check_vma=False,
    )
```

```python
import math

import jax
import jax.numpy as jnp
from jax import lax
from jax.sharding import PartitionSpec as P

STEPS = 4
LAGS = 256
NFFT = 2400
FIRST_BIN = 60

PART_ORDERS = (
    ((0, 1, 3, 5, 2), 4),
    ((0, 3, 5, 1, 4), 2),
    ((0, 5, 1, 3, 2), 4),
)


def swap(value, bit, size):
    return lax.ppermute(value, "sta", [(i, i ^ (1 << bit)) for i in range(size)])


def halve(buf, order, me, size):
    for bit in order:
        v = (me >> bit) & 1
        keep = lax.dynamic_index_in_dim(buf, v, 0, keepdims=False)
        send = lax.dynamic_index_in_dim(buf, 1 - v, 0, keepdims=False)
        buf = keep + swap(send, bit, size)
    return buf


def double(piece, order, me, size):
    buf = piece
    for bit in reversed(order):
        v = (me >> bit) & 1
        other = swap(buf, bit, size)
        lo = jnp.where(v == 1, other, buf)
        hi = jnp.where(v == 1, buf, other)
        buf = jnp.stack([lo, hi], axis=0)
    return buf


def broadcast_blocks(whitened, owner_order):
    size = lax.axis_size("sta")
    me = lax.axis_index("sta")
    masked = jnp.stack(
        [jnp.where(me == owner_order[s], whitened, jnp.zeros_like(whitened)) for s in range(STEPS)]
    )
    shape = masked.shape
    planes = masked.reshape((-1,) + shape[-2:])
    parts = len(PART_ORDERS)
    per_part = planes.shape[0] // parts
    outs = []
    for p, (order, exch) in enumerate(PART_ORDERS):
        buf = planes[p * per_part:(p + 1) * per_part]
        buf = buf.reshape((2,) * len(order) + (-1,) + shape[-2:])
        piece = halve(buf, order, me, size)
        piece = piece + swap(piece, exch, size)
        full = double(piece, order, me, size)
        outs.append(full.reshape((per_part,) + shape[-2:]))
    return jnp.concatenate(outs, axis=0).reshape(shape)


def whiten(spectra):
    values = spectra.astype(jnp.float32)
    energy = jnp.mean(values * values, axis=(2, 4), keepdims=True)
    return (values / jnp.sqrt(energy + 1e-06)).astype(jnp.bfloat16)


def lag_table(bins, lag_count):
    freq_index = FIRST_BIN + lax.iota(jnp.int32, bins)
    lag_index = lax.iota(jnp.int32, lag_count) - lag_count // 2
    phase = freq_index[:, None] * lag_index[None, :] % NFFT
    angle = phase.astype(jnp.float32) * (2.0 * math.pi / NFFT)
    return jnp.stack([jnp.cos(angle), -jnp.sin(angle)]).astype(jnp.bfloat16)


def split_local(local):
    wide = local.astype(jnp.float32)
    return jnp.stack([wide[:, 0], wide[:, 1], wide[:, 0] - wide[:, 1]])


def day_correlation(owner, local_parts, day_valid, lag_grid, stack_scale):
    masked = (owner * day_valid.astype(jnp.bfloat16)[:, None, None, None]).astype(jnp.float32)
    owner_parts = jnp.stack([masked[:, 0], masked[:, 1], masked[:, 0] + masked[:, 1]])
    p, q, r = jnp.sum(owner_parts[:, :, :, None, :] * local_parts[:, :, None, :, :], axis=1)
    cross = jnp.concatenate([p + q, (r - p) + q], axis=-1)
    cross = (cross * stack_scale).astype(jnp.bfloat16)
    a, b, kf = cross.shape
    lag_sums = jnp.dot(
        cross.reshape(a * b, kf), lag_grid.reshape(kf, -1), preferred_element_type=jnp.float32
    ).reshape(a, b, -1)
    return lag_sums * (1.0 / math.sqrt(kf // 2))


def body(spectra, window_valid, owner_order):
    day_index = lax.axis_index("day")
    whitened = whiten(spectra)[0]
    lag_grid = lag_table(whitened.shape[3], LAGS)
    stack_scale = 1.0 / math.sqrt(lax.axis_size("day") * whitened.shape[0])
    own_valid = lax.dynamic_index_in_dim(window_valid, day_index, 0, keepdims=False)
    owners = broadcast_blocks(whitened, owner_order)
    half = whitened.shape[2] // lax.axis_size("day")
    partner = [(0, 1), (1, 0)]
    results = []
    local = split_local(whitened)
    for step_index in range(STEPS):
        if results:
            local, results[-1] = lax.optimization_barrier((local, results[-1]))
        owner = owners[step_index]
        theirs = lax.dynamic_slice_in_dim(owner, (1 - day_index) * half, half, 2)
        sent = day_correlation(theirs, local, own_valid, lag_grid, stack_scale).astype(jnp.bfloat16)
        sent, local = lax.optimization_barrier((sent, local))
        received = lax.ppermute(sent, "day", partner)
        mine = lax.dynamic_slice_in_dim(owner, day_index * half, half, 2)
        kept = day_correlation(mine, local, own_valid, lag_grid, stack_scale).astype(jnp.bfloat16)
        kept, local = lax.optimization_barrier((kept, local))
        share = (kept.astype(jnp.float32) + received.astype(jnp.float32)).astype(jnp.bfloat16)
        results.append(share)
    return jnp.stack(results)


def solution(mesh):
    return jax.shard_map(
        body,
        mesh=mesh,
        in_specs=(P("day", None, None, "sta", None), P(), P()),
        out_specs=P(None, "day", "sta", None),
        check_vma=False,
    )
```

```python
import math

import jax
import jax.numpy as jnp
from jax import lax
from jax.sharding import PartitionSpec as P

STEPS = 4
LAGS = 256
NFFT = 2400
FIRST_BIN = 60

PART_ORDERS = (
    (0, 1, 3, 5, 2, 4),
    (0, 3, 5, 1, 4, 2),
)


def swap(value, bit, size):
    return lax.ppermute(value, "sta", [(i, i ^ (1 << bit)) for i in range(size)])


def halve(buf, order, me, size):
    for bit in order:
        v = (me >> bit) & 1
        keep = lax.dynamic_index_in_dim(buf, v, 0, keepdims=False)
        send = lax.dynamic_index_in_dim(buf, 1 - v, 0, keepdims=False)
        buf = keep + swap(send, bit, size)
    return buf


def double(piece, order, me, size):
    buf = piece
    for bit in reversed(order):
        v = (me >> bit) & 1
        other = swap(buf, bit, size)
        lo = jnp.where(v == 1, other, buf)
        hi = jnp.where(v == 1, buf, other)
        buf = jnp.stack([lo, hi], axis=0)
    return buf


def broadcast_blocks(whitened, owner_order):
    size = lax.axis_size("sta")
    me = lax.axis_index("sta")
    masked = jnp.stack(
        [jnp.where(me == owner_order[s], whitened, jnp.zeros_like(whitened)) for s in range(STEPS)]
    )
    shape = masked.shape
    planes = masked.reshape((-1,) + shape[-2:])
    parts = len(PART_ORDERS)
    per_part = planes.shape[0] // parts
    split = 0
    while per_part % (2 << split) == 0 and split < len(PART_ORDERS[0]):
        split += 1
    outs = []
    for p, order in enumerate(PART_ORDERS):
        halving, exchange = order[:split], order[split:]
        buf = planes[p * per_part:(p + 1) * per_part]
        buf = buf.reshape((2,) * split + (-1,) + shape[-2:])
        piece = halve(buf, halving, me, size)
        for bit in exchange:
            piece = piece + swap(piece, bit, size)
        full = double(piece, halving, me, size)
        outs.append(full.reshape((per_part,) + shape[-2:]))
    return jnp.concatenate(outs, axis=0).reshape(shape)


def whiten(spectra):
    values = spectra.astype(jnp.float32)
    energy = jnp.mean(values * values, axis=(2, 4), keepdims=True)
    return (values / jnp.sqrt(energy + 1e-06)).astype(jnp.bfloat16)


def lag_table(bins, lag_count):
    freq_index = FIRST_BIN + lax.iota(jnp.int32, bins)
    lag_index = lax.iota(jnp.int32, lag_count) - lag_count // 2
    phase = freq_index[:, None] * lag_index[None, :] % NFFT
    angle = phase.astype(jnp.float32) * (2.0 * math.pi / NFFT)
    return jnp.stack([jnp.cos(angle), -jnp.sin(angle)]).astype(jnp.bfloat16)


def split_local(local):
    wide = local.astype(jnp.float32)
    return jnp.stack([wide[:, 0], wide[:, 1], wide[:, 0] - wide[:, 1]])


def day_correlation(owner, local_parts, day_valid, lag_grid, stack_scale):
    masked = (owner * day_valid.astype(jnp.bfloat16)[:, None, None, None]).astype(jnp.float32)
    owner_parts = jnp.stack([masked[:, 0], masked[:, 1], masked[:, 0] + masked[:, 1]])
    p, q, r = jnp.sum(owner_parts[:, :, :, None, :] * local_parts[:, :, None, :, :], axis=1)
    cross = jnp.concatenate([p + q, (r - p) + q], axis=-1)
    cross = (cross * stack_scale).astype(jnp.bfloat16)
    a, b, kf = cross.shape
    lag_sums = jnp.dot(
        cross.reshape(a * b, kf), lag_grid.reshape(kf, -1), preferred_element_type=jnp.float32
    ).reshape(a, b, -1)
    return lag_sums * (1.0 / math.sqrt(kf // 2))


def body(spectra, window_valid, owner_order):
    day_index = lax.axis_index("day")
    whitened = whiten(spectra)[0]
    lag_grid = lag_table(whitened.shape[3], LAGS)
    stack_scale = 1.0 / math.sqrt(lax.axis_size("day") * whitened.shape[0])
    own_valid = lax.dynamic_index_in_dim(window_valid, day_index, 0, keepdims=False)
    owners = broadcast_blocks(whitened, owner_order)
    half = whitened.shape[2] // lax.axis_size("day")
    partner = [(0, 1), (1, 0)]
    results = []
    local = split_local(whitened)
    for step_index in range(STEPS):
        if results:
            local, results[-1] = lax.optimization_barrier((local, results[-1]))
        owner = owners[step_index]
        theirs = lax.dynamic_slice_in_dim(owner, (1 - day_index) * half, half, 2)
        sent = day_correlation(theirs, local, own_valid, lag_grid, stack_scale).astype(jnp.bfloat16)
        sent, local = lax.optimization_barrier((sent, local))
        received = lax.ppermute(sent, "day", partner)
        mine = lax.dynamic_slice_in_dim(owner, day_index * half, half, 2)
        kept = day_correlation(mine, local, own_valid, lag_grid, stack_scale).astype(jnp.bfloat16)
        kept, local = lax.optimization_barrier((kept, local))
        share = (kept.astype(jnp.float32) + received.astype(jnp.float32)).astype(jnp.bfloat16)
        results.append(share)
    return jnp.stack(results)


def solution(mesh):
    return jax.shard_map(
        body,
        mesh=mesh,
        in_specs=(P("day", None, None, "sta", None), P(), P()),
        out_specs=P(None, "day", "sta", None),
        check_vma=False,
    )
```

```python
import math

import jax
import jax.numpy as jnp
from jax import lax
from jax.sharding import PartitionSpec as P

STEPS = 4
LAGS = 256
NFFT = 2400
FIRST_BIN = 60

PART_ORDERS = (
    ((0, 1, 3, 5, 2), 4),
    ((0, 3, 5, 1, 4), 2),
    ((0, 5, 1, 3, 2), 4),
)


def swap(value, bit, size):
    return lax.ppermute(value, "sta", [(i, i ^ (1 << bit)) for i in range(size)])


def halve(buf, order, me, size):
    for bit in order:
        v = (me >> bit) & 1
        keep = lax.dynamic_index_in_dim(buf, v, 0, keepdims=False)
        send = lax.dynamic_index_in_dim(buf, 1 - v, 0, keepdims=False)
        buf = keep + swap(send, bit, size)
    return buf


def double(piece, order, me, size):
    buf = piece
    for bit in reversed(order):
        v = (me >> bit) & 1
        other = swap(buf, bit, size)
        lo = jnp.where(v == 1, other, buf)
        hi = jnp.where(v == 1, buf, other)
        buf = jnp.stack([lo, hi], axis=0)
    return buf


def broadcast_blocks(whitened, owner_order):
    size = lax.axis_size("sta")
    me = lax.axis_index("sta")
    masked = jnp.stack(
        [jnp.where(me == owner_order[s], whitened, jnp.zeros_like(whitened)) for s in range(STEPS)]
    )
    shape = masked.shape
    planes = masked.reshape((-1,) + shape[-2:])
    parts = len(PART_ORDERS)
    per_part = planes.shape[0] // parts
    outs = []
    for p, (order, exch) in enumerate(PART_ORDERS):
        buf = planes[p * per_part:(p + 1) * per_part]
        buf = buf.reshape((2,) * len(order) + (-1,) + shape[-2:])
        piece = halve(buf, order, me, size)
        piece = piece + swap(piece, exch, size)
        full = double(piece, order, me, size)
        outs.append(full.reshape((per_part,) + shape[-2:]))
    return jnp.concatenate(outs, axis=0).reshape(shape)


def whiten(spectra):
    values = spectra.astype(jnp.float32)
    energy = jnp.mean(values * values, axis=(2, 4), keepdims=True)
    return (values / jnp.sqrt(energy + 1e-06)).astype(jnp.bfloat16)


def lag_table(bins, lag_count):
    freq_index = FIRST_BIN + lax.iota(jnp.int32, bins)
    lag_index = lax.iota(jnp.int32, lag_count) - lag_count // 2
    phase = freq_index[:, None] * lag_index[None, :] % NFFT
    angle = phase.astype(jnp.float32) * (2.0 * math.pi / NFFT)
    return jnp.stack([jnp.cos(angle), -jnp.sin(angle)]).astype(jnp.bfloat16)


def split_local(local):
    wide = local.astype(jnp.float32)
    return jnp.stack([wide[:, 0], wide[:, 1], wide[:, 0] - wide[:, 1]])


def owner_parts(owners, day_valid):
    masked = (owners * day_valid.astype(jnp.bfloat16)[None, :, None, None, None]).astype(jnp.float32)
    return jnp.stack([masked[:, :, 0], masked[:, :, 1], masked[:, :, 0] + masked[:, :, 1]], axis=1)


def day_correlation(parts_o, local_parts, lag_grid, stack_scale):
    p, q, r = jnp.sum(parts_o[:, :, :, None, :] * local_parts[:, :, None, :, :], axis=1)
    cross = jnp.concatenate([p + q, (r - p) + q], axis=-1)
    cross = (cross * stack_scale).astype(jnp.bfloat16)
    a, b, kf = cross.shape
    lag_sums = jnp.dot(
        cross.reshape(a * b, kf), lag_grid.reshape(kf, -1), preferred_element_type=jnp.float32
    ).reshape(a, b, -1)
    return lag_sums * (1.0 / math.sqrt(kf // 2))


def body(spectra, window_valid, owner_order):
    day_index = lax.axis_index("day")
    whitened = whiten(spectra)[0]
    lag_grid = lag_table(whitened.shape[3], LAGS)
    stack_scale = 1.0 / math.sqrt(lax.axis_size("day") * whitened.shape[0])
    own_valid = lax.dynamic_index_in_dim(window_valid, day_index, 0, keepdims=False)
    owners = owner_parts(broadcast_blocks(whitened, owner_order), own_valid)
    half = whitened.shape[2] // lax.axis_size("day")
    partner = [(0, 1), (1, 0)]
    results = []
    local = split_local(whitened)
    for step_index in range(STEPS):
        if results:
            local, results[-1] = lax.optimization_barrier((local, results[-1]))
        owner = owners[step_index]
        theirs = lax.dynamic_slice_in_dim(owner, (1 - day_index) * half, half, 2)
        sent = day_correlation(theirs, local, lag_grid, stack_scale).astype(jnp.bfloat16)
        sent, local = lax.optimization_barrier((sent, local))
        received = lax.ppermute(sent, "day", partner)
        mine = lax.dynamic_slice_in_dim(owner, day_index * half, half, 2)
        kept = day_correlation(mine, local, lag_grid, stack_scale).astype(jnp.bfloat16)
        kept, local = lax.optimization_barrier((kept, local))
        share = (kept.astype(jnp.float32) + received.astype(jnp.float32)).astype(jnp.bfloat16)
        results.append(share)
    return jnp.stack(results)


def solution(mesh):
    return jax.shard_map(
        body,
        mesh=mesh,
        in_specs=(P("day", None, None, "sta", None), P(), P()),
        out_specs=P(None, "day", "sta", None),
        check_vma=False,
    )
```

```python
import math

import jax
import jax.numpy as jnp
from jax import lax
from jax.sharding import PartitionSpec as P

STEPS = 4
LAGS = 256
NFFT = 2400
FIRST_BIN = 60

CORE_BIT = 0
PART_ORDERS = (
    (1, 3, 5, 2, 4),
    (3, 5, 1, 4, 2),
    (5, 1, 3, 2, 4),
)


def swap(value, bit, size):
    return lax.ppermute(value, "sta", [(i, i ^ (1 << bit)) for i in range(size)])


def halve(buf, order, me, size):
    for bit in order:
        v = (me >> bit) & 1
        keep = lax.dynamic_index_in_dim(buf, v, 0, keepdims=False)
        send = lax.dynamic_index_in_dim(buf, 1 - v, 0, keepdims=False)
        buf = keep + swap(send, bit, size)
    return buf


def double(piece, order, me, size):
    buf = piece
    for bit in reversed(order):
        v = (me >> bit) & 1
        other = swap(buf, bit, size)
        lo = jnp.where(v == 1, other, buf)
        hi = jnp.where(v == 1, buf, other)
        buf = jnp.stack([lo, hi], axis=0)
    return buf


def broadcast_blocks(whitened, owner_order):
    size = lax.axis_size("sta")
    me = lax.axis_index("sta")
    masked = jnp.stack(
        [jnp.where(me == owner_order[s], whitened, jnp.zeros_like(whitened)) for s in range(STEPS)]
    )
    shape = masked.shape
    planes = masked.reshape((2, -1) + shape[-2:])
    half = halve(planes, (CORE_BIT,), me, size)
    parts = len(PART_ORDERS)
    per_part = half.shape[0] // parts
    split = 0
    while per_part % (2 << split) == 0 and split < len(PART_ORDERS[0]):
        split += 1
    outs = []
    for p, order in enumerate(PART_ORDERS):
        halving, exchange = order[:split], order[split:]
        buf = half[p * per_part:(p + 1) * per_part]
        buf = buf.reshape((2,) * split + (-1,) + shape[-2:])
        piece = halve(buf, halving, me, size)
        for bit in exchange:
            piece = piece + swap(piece, bit, size)
        full = double(piece, halving, me, size)
        outs.append(full.reshape((per_part,) + shape[-2:]))
    whole = double(jnp.concatenate(outs, axis=0), (CORE_BIT,), me, size)
    return whole.reshape(shape)


def whiten(spectra):
    values = spectra.astype(jnp.float32)
    energy = jnp.mean(values * values, axis=(2, 4), keepdims=True)
    return (values / jnp.sqrt(energy + 1e-06)).astype(jnp.bfloat16)


def lag_table(bins, lag_count):
    freq_index = FIRST_BIN + lax.iota(jnp.int32, bins)
    lag_index = lax.iota(jnp.int32, lag_count) - lag_count // 2
    phase = freq_index[:, None] * lag_index[None, :] % NFFT
    angle = phase.astype(jnp.float32) * (2.0 * math.pi / NFFT)
    return jnp.stack([jnp.cos(angle), -jnp.sin(angle)]).astype(jnp.bfloat16)


def split_local(local):
    wide = local.astype(jnp.float32)
    return jnp.stack([wide[:, 0], wide[:, 1], wide[:, 0] - wide[:, 1]])


def day_correlation(owner, local_parts, day_valid, lag_grid, stack_scale):
    masked = (owner * day_valid.astype(jnp.bfloat16)[:, None, None, None]).astype(jnp.float32)
    owner_parts = jnp.stack([masked[:, 0], masked[:, 1], masked[:, 0] + masked[:, 1]])
    p, q, r = jnp.sum(owner_parts[:, :, :, None, :] * local_parts[:, :, None, :, :], axis=1)
    cross = jnp.concatenate([p + q, (r - p) + q], axis=-1)
    cross = (cross * stack_scale).astype(jnp.bfloat16)
    a, b, kf = cross.shape
    lag_sums = jnp.dot(
        cross.reshape(a * b, kf), lag_grid.reshape(kf, -1), preferred_element_type=jnp.float32
    ).reshape(a, b, -1)
    return lag_sums * (1.0 / math.sqrt(kf // 2))


def body(spectra, window_valid, owner_order):
    day_index = lax.axis_index("day")
    whitened = whiten(spectra)[0]
    lag_grid = lag_table(whitened.shape[3], LAGS)
    stack_scale = 1.0 / math.sqrt(lax.axis_size("day") * whitened.shape[0])
    own_valid = lax.dynamic_index_in_dim(window_valid, day_index, 0, keepdims=False)
    owners = broadcast_blocks(whitened, owner_order)
    half = whitened.shape[2] // lax.axis_size("day")
    partner = [(0, 1), (1, 0)]
    results = []
    local = split_local(whitened)
    for step_index in range(STEPS):
        if results:
            local, results[-1] = lax.optimization_barrier((local, results[-1]))
        owner = owners[step_index]
        theirs = lax.dynamic_slice_in_dim(owner, (1 - day_index) * half, half, 2)
        sent = day_correlation(theirs, local, own_valid, lag_grid, stack_scale).astype(jnp.bfloat16)
        sent, local = lax.optimization_barrier((sent, local))
        received = lax.ppermute(sent, "day", partner)
        mine = lax.dynamic_slice_in_dim(owner, day_index * half, half, 2)
        kept = day_correlation(mine, local, own_valid, lag_grid, stack_scale).astype(jnp.bfloat16)
        kept, local = lax.optimization_barrier((kept, local))
        share = (kept.astype(jnp.float32) + received.astype(jnp.float32)).astype(jnp.bfloat16)
        results.append(share)
    return jnp.stack(results)


def solution(mesh):
    return jax.shard_map(
        body,
        mesh=mesh,
        in_specs=(P("day", None, None, "sta", None), P(), P()),
        out_specs=P(None, "day", "sta", None),
        check_vma=False,
    )
```

```python
import math

import jax
import jax.numpy as jnp
from jax import lax
from jax.sharding import PartitionSpec as P

STEPS = 4
LAGS = 256
NFFT = 2400
FIRST_BIN = 60

PART_ORDERS = (
    ((0, 1, 3, 5, 2), 4),
    ((0, 3, 5, 1, 4), 2),
    ((0, 5, 1, 3, 2), 4),
)


def swap(value, bit, size):
    return lax.ppermute(value, "sta", [(i, i ^ (1 << bit)) for i in range(size)])


def halve(buf, order, me, size):
    for bit in order:
        v = (me >> bit) & 1
        keep = lax.dynamic_index_in_dim(buf, v, 0, keepdims=False)
        send = lax.dynamic_index_in_dim(buf, 1 - v, 0, keepdims=False)
        buf = keep + swap(send, bit, size)
    return buf


def double(piece, order, me, size):
    buf = piece
    for bit in reversed(order):
        v = (me >> bit) & 1
        other = swap(buf, bit, size)
        lo = jnp.where(v == 1, other, buf)
        hi = jnp.where(v == 1, buf, other)
        buf = jnp.stack([lo, hi], axis=0)
    return buf


def broadcast_blocks(whitened, owner_order):
    size = lax.axis_size("sta")
    me = lax.axis_index("sta")
    masked = jnp.stack(
        [jnp.where(me == owner_order[s], whitened, jnp.zeros_like(whitened)) for s in range(STEPS)]
    )
    shape = masked.shape
    planes = masked.reshape((-1,) + shape[-2:])
    parts = len(PART_ORDERS)
    per_part = planes.shape[0] // parts
    outs = []
    for p, (order, exch) in enumerate(PART_ORDERS):
        buf = planes[p * per_part:(p + 1) * per_part]
        buf = buf.reshape((2,) * len(order) + (-1,) + shape[-2:])
        piece = halve(buf, order, me, size)
        piece = piece + swap(piece, exch, size)
        full = double(piece, order, me, size)
        outs.append(full.reshape((per_part,) + shape[-2:]))
    return jnp.concatenate(outs, axis=0).reshape(shape)


def whiten(spectra):
    values = spectra.astype(jnp.float32)
    energy = jnp.mean(values * values, axis=(2, 4), keepdims=True)
    return (values / jnp.sqrt(energy + 1e-06)).astype(jnp.bfloat16)


def lag_table(bins, lag_count):
    freq_index = FIRST_BIN + lax.iota(jnp.int32, bins)
    lag_index = lax.iota(jnp.int32, lag_count) - lag_count // 2
    phase = freq_index[:, None] * lag_index[None, :] % NFFT
    angle = phase.astype(jnp.float32) * (2.0 * math.pi / NFFT)
    return jnp.stack([jnp.cos(angle), -jnp.sin(angle)]).astype(jnp.bfloat16)


def split_local(local, day_valid):
    wide = (local * day_valid.astype(jnp.bfloat16)[:, None, None, None]).astype(jnp.float32)
    return jnp.stack([wide[:, 0], wide[:, 1], wide[:, 0] - wide[:, 1]])


def day_correlation(owner, local_parts, day_valid, lag_grid, stack_scale):
    masked = owner.astype(jnp.float32)
    owner_parts = jnp.stack([masked[:, 0], masked[:, 1], masked[:, 0] + masked[:, 1]])
    p, q, r = jnp.sum(owner_parts[:, :, :, None, :] * local_parts[:, :, None, :, :], axis=1)
    cross = jnp.concatenate([p + q, (r - p) + q], axis=-1)
    cross = (cross * stack_scale).astype(jnp.bfloat16)
    a, b, kf = cross.shape
    lag_sums = jnp.dot(
        cross.reshape(a * b, kf), lag_grid.reshape(kf, -1), preferred_element_type=jnp.float32
    ).reshape(a, b, -1)
    return lag_sums * (1.0 / math.sqrt(kf // 2))


def body(spectra, window_valid, owner_order):
    day_index = lax.axis_index("day")
    whitened = whiten(spectra)[0]
    lag_grid = lag_table(whitened.shape[3], LAGS)
    stack_scale = 1.0 / math.sqrt(lax.axis_size("day") * whitened.shape[0])
    own_valid = lax.dynamic_index_in_dim(window_valid, day_index, 0, keepdims=False)
    owners = broadcast_blocks(whitened, owner_order)
    half = whitened.shape[2] // lax.axis_size("day")
    partner = [(0, 1), (1, 0)]
    results = []
    local = split_local(whitened, own_valid)
    for step_index in range(STEPS):
        if results:
            local, results[-1] = lax.optimization_barrier((local, results[-1]))
        owner = owners[step_index]
        theirs = lax.dynamic_slice_in_dim(owner, (1 - day_index) * half, half, 2)
        sent = day_correlation(theirs, local, own_valid, lag_grid, stack_scale).astype(jnp.bfloat16)
        sent, local = lax.optimization_barrier((sent, local))
        received = lax.ppermute(sent, "day", partner)
        mine = lax.dynamic_slice_in_dim(owner, day_index * half, half, 2)
        kept = day_correlation(mine, local, own_valid, lag_grid, stack_scale).astype(jnp.bfloat16)
        kept, local = lax.optimization_barrier((kept, local))
        share = (kept.astype(jnp.float32) + received.astype(jnp.float32)).astype(jnp.bfloat16)
        results.append(share)
    return jnp.stack(results)


def solution(mesh):
    return jax.shard_map(
        body,
        mesh=mesh,
        in_specs=(P("day", None, None, "sta", None), P(), P()),
        out_specs=P(None, "day", "sta", None),
        check_vma=False,
    )
```
